256 devices in a mesh: ctx: 32 (over z, y_hi, core), head: 8 (over x, y_lo).
Axes of the slice: x: 4, y: 4 (y_hi: 2, y_lo: 2; y = y_hi * 2 + y_lo), z: 8, core: 2. Of those that a mesh axis runs over, the one named last changes fastest.
Arguments:
- doc_lengths: int32 [16], replicated, may hold values from 1 to 4352, 8192 in all
- queries: bfloat16 [2, 8192, 16384], P(None, 'ctx', 'head'), may hold values from -120 to 120
- rotated_key_rows: bfloat16 [2, 8192, 1024], P(None, ('ctx', 'head')), may hold values from -6 to 6
- value_row_matrix: bfloat16 [2, 8192, 1024], P(None, ('ctx', 'head')), may hold values from -6 to 6
Outputs:
- attended: bfloat16 [2, 8192, 16384], P(None, 'ctx', 'head')
The draws below stay inside these ranges and needn't reach their ends.
All inputs are finite; a program needn't handle non-finite values.
Results may differ from the reference program's by a relative error of at most 0.003.
Values may be sent and summed in bfloat16 or wider, within the bound.
No kernel may reach another device: no remote copies, remote signals or barrier semaphores. Data moves between devices by JAX's collectives and lax.ppermute only.
A program may use at most 64 MiB of HBM per device.

```python
import math
import jax
import jax.numpy as jnp
import numpy as np
from jax import lax

QUERY_HEAD_COUNT = 128
VALUE_KEY_HEADS = 8
HEAD_SIZE = 128
TOK_DEV = 256
PACKED_TOKENS = 8192
NDOCS = 16
LONGEST = 4352


def shared_draw(key):
    base_angle = jax.random.fold_in(key, 31)
    unrotated_keys = jax.random.truncated_normal(jax.random.fold_in(base_angle, 1), -6.0, 6.0, (2, PACKED_TOKENS, VALUE_KEY_HEADS * HEAD_SIZE), jnp.float32)
    return unrotated_keys


def final_keys(key):
    unrotated_keys = shared_draw(key)
    return unrotated_keys


def draw_rotated_key_rows(key, part):
    return final_keys(key).astype(jnp.bfloat16)


def draw_queries(key, part):
    base_angle = jax.random.fold_in(key, 31)
    raw_queries = jax.random.truncated_normal(jax.random.fold_in(base_angle, 4), -6.0, 6.0, (2, PACKED_TOKENS, QUERY_HEAD_COUNT * HEAD_SIZE), jnp.float32)
    return raw_queries.astype(jnp.bfloat16)


def draw_value_row_matrix(key, part):
    base_angle = jax.random.fold_in(key, 57)
    random_noise = jax.random.truncated_normal(jax.random.fold_in(base_angle, 1), -3.5, 3.5, (2, PACKED_TOKENS, VALUE_KEY_HEADS * HEAD_SIZE), jnp.float32)
    rotary_angle = jax.random.uniform(jax.random.fold_in(base_angle, 2), (VALUE_KEY_HEADS * HEAD_SIZE,), jnp.float32, 0.0, 2.0 * math.pi)
    position = jnp.arange(PACKED_TOKENS, dtype=jnp.float32)
    trend = 2.0 * jnp.sin(2.0 * math.pi * position[:, None] / (3.0 * TOK_DEV) + rotary_angle[None, :])
    return (random_noise + trend[None, :, :]).astype(jnp.bfloat16)


def length_profile(number_of, total, limit, slope):
    portions = [(1 << 20) // math.isqrt(standing ** slope) + 1 for standing in range(2, number_of + 1)]
    rest, counts = total - limit - (number_of - 1), [1] * (number_of - 1)
    while rest > 0:
        free = [i for i in range(number_of - 1) if counts[i] < limit]
        pool, left = sum([portions[i] for i in free]), rest
        for i in free:
            addition = min(limit - counts[i], max(1, left * portions[i] // pool), rest)
            counts[i] = counts[i] + addition
            rest = rest - addition
    return np.array([limit] + counts)


def uneven(stream_key, count, total, bound, skew):
    if count == 2:
        one = jax.random.randint(stream_key, (), max(1, total - bound), min(bound, total - 1) + 1)
        return jnp.stack([one, total - one])
    sizes = jnp.asarray(length_profile(count, total, bound, skew), jnp.int32)
    twos = (count - 1) // 2
    giver, taker = sizes[1:1 + 2 * twos:2], sizes[2:2 + 2 * twos:2]
    margin = jnp.minimum(giver - 1, bound - taker)
    shifted = jax.random.randint(jax.random.fold_in(stream_key, 1), (twos,), 0, 1 << 20) % (margin + 1)
    sizes = sizes.at[1:1 + 2 * twos:2].set(giver - shifted).at[2:2 + 2 * twos:2].set(taker + shifted)
    return sizes[jax.random.permutation(jax.random.fold_in(stream_key, 2), count)]


def setup_inputs(seed: int = 0) -> dict:
    arg_keys = jax.random.split(jax.random.key(seed), 5)
    doc_lengths = uneven(arg_keys[0], NDOCS, PACKED_TOKENS, LONGEST, 2).astype(jnp.int32)
    queries = draw_queries(jax.random.fold_in(arg_keys[4], 71), 0)
    rotated_key_rows = draw_rotated_key_rows(jax.random.fold_in(arg_keys[4], 71), 0)
    value_row_matrix = draw_value_row_matrix(jax.random.fold_in(arg_keys[4], 71), 0)
    return dict(doc_lengths=doc_lengths, queries=queries, rotated_key_rows=rotated_key_rows, value_row_matrix=value_row_matrix)


NEG_FILL = -1.0e30


def doc_index(positions, doc_ends):
    return jnp.sum((positions[:, None] >= doc_ends[None, :]).astype(jnp.int32), axis=1)


def reference(doc_lengths, queries, rotated_key_rows, value_row_matrix):
    doc_ends = jnp.cumsum(doc_lengths).astype(jnp.int32)
    group_width = QUERY_HEAD_COUNT // VALUE_KEY_HEADS
    span = min(LONGEST + TOK_DEV, PACKED_TOKENS)
    block_count = PACKED_TOKENS // TOK_DEV
    query_tensor = queries.reshape(2, PACKED_TOKENS, VALUE_KEY_HEADS, group_width, HEAD_SIZE)
    key_tensor = rotated_key_rows.reshape(2, PACKED_TOKENS, VALUE_KEY_HEADS, HEAD_SIZE)
    value_tensor = value_row_matrix.reshape(2, PACKED_TOKENS, VALUE_KEY_HEADS, HEAD_SIZE)

    def one_block(block_index):
        query_start = (block_index * TOK_DEV).astype(jnp.int32)
        key_start = jnp.maximum(query_start + TOK_DEV - span, 0).astype(jnp.int32)
        query_block = lax.dynamic_slice_in_dim(query_tensor, query_start, TOK_DEV, 1)
        key_block = lax.dynamic_slice_in_dim(key_tensor, key_start, span, 1)
        value_block = lax.dynamic_slice_in_dim(value_tensor, key_start, span, 1)
        query_pos = query_start + jnp.arange(TOK_DEV, dtype=jnp.int32)
        key_pos = key_start + jnp.arange(span, dtype=jnp.int32)
        allowed = (doc_index(key_pos, doc_ends)[None, :] == doc_index(query_pos, doc_ends)[:, None]) & (key_pos[None, :] <= query_pos[:, None])

        def single_head(head_index):
            query_head = lax.dynamic_index_in_dim(query_block, head_index, 2, keepdims=False).astype(jnp.float32)
            key_head = lax.dynamic_index_in_dim(key_block, head_index, 2, keepdims=False).astype(jnp.float32)
            value_head = lax.dynamic_index_in_dim(value_block, head_index, 2, keepdims=False).astype(jnp.float32)
            scores = jnp.einsum("bqgd,bsd->bgqs", query_head, key_head) * (HEAD_SIZE ** -0.5)
            scores = jnp.where(allowed, scores, NEG_FILL)
            peak = jnp.max(scores, axis=-1, keepdims=True)
            probs = jnp.where(allowed, jnp.exp(scores - peak), 0.0)
            total = jnp.sum(probs, axis=-1)
            rounded = lax.optimization_barrier(probs.astype(jnp.bfloat16)).astype(jnp.float32)
            accum = jnp.einsum("bgqs,bsd->bgqd", rounded, value_head)
            return accum / total[..., None]

        head_outputs = lax.map(single_head, jnp.arange(VALUE_KEY_HEADS, dtype=jnp.int32))
        merged = jnp.transpose(head_outputs, (1, 3, 0, 2, 4)).reshape(2, TOK_DEV, QUERY_HEAD_COUNT * HEAD_SIZE)
        return merged.astype(jnp.bfloat16)

    blocks = lax.map(one_block, jnp.arange(block_count, dtype=jnp.int32))
    return jnp.transpose(blocks, (1, 0, 2, 3)).reshape(2, PACKED_TOKENS, QUERY_HEAD_COUNT * HEAD_SIZE)
```

```python
import functools

import jax
import jax.numpy as jnp
from jax import lax
from jax.experimental import pallas as pl
from jax.experimental.pallas import tpu as pltpu
from jax.sharding import PartitionSpec as P

HEAD_SIZE = 128
LONGEST = 4352
NEG_FILL = -1e30

ROW_TILE = 1024
KEY_TILE = 512


def attend_kernel(first_ref, last_ref, lo_ref, hi_ref, q_ref, k_ref, v_ref, o_ref,
                  peak_sc, total_sc, accum_sc, *, key_tile, steps, scale):
    tile = pl.program_id(1)
    step = pl.program_id(2)
    block = first_ref[tile] + step

    @pl.when(step == 0)
    def _():
        peak_sc[...] = jnp.full(peak_sc.shape, NEG_FILL, jnp.float32)
        total_sc[...] = jnp.zeros(total_sc.shape, jnp.float32)
        accum_sc[...] = jnp.zeros(accum_sc.shape, jnp.float32)

    @pl.when(block <= last_ref[tile])
    def _():
        scores = lax.dot_general(
            q_ref[0], k_ref[0], (((1,), (1,)), ((), ())),
            preferred_element_type=jnp.float32) * scale
        key_pos = block * key_tile + lax.broadcasted_iota(jnp.int32, (1, key_tile), 1)
        allowed = (key_pos >= lo_ref[...]) & (key_pos <= hi_ref[...])
        scores = jnp.where(allowed, scores, NEG_FILL)
        peak_old = peak_sc[...]
        peak_new = jnp.maximum(peak_old, jnp.max(scores, axis=-1, keepdims=True))
        probs = jnp.where(allowed, jnp.exp(scores - peak_new), 0.0)
        factor = jnp.exp(peak_old - peak_new)
        total_sc[...] = total_sc[...] * factor + jnp.sum(probs, axis=-1, keepdims=True)
        accum_sc[...] = accum_sc[...] * factor + lax.dot_general(
            probs.astype(jnp.bfloat16), v_ref[0], (((1,), (0,)), ((), ())),
            preferred_element_type=jnp.float32)
        peak_sc[...] = peak_new

    @pl.when(step == steps - 1)
    def _():
        o_ref[0] = (accum_sc[...] / total_sc[...]).astype(o_ref.dtype)


def attend(queries, kv, first, last, lo, hi):
    models, rows, head_dim = queries.shape
    key_count = kv.shape[1]
    row_tile = min(ROW_TILE, rows)
    key_tile = min(KEY_TILE, key_count)
    tiles = rows // row_tile
    steps = min(key_count // key_tile, (LONGEST + row_tile - 2) // key_tile + 2)

    def key_map(b, t, j, first_ref, last_ref):
        return (b, jnp.minimum(first_ref[t] + j, last_ref[t]), 0)

    def value_map(b, t, j, first_ref, last_ref):
        return (b, jnp.minimum(first_ref[t] + j, last_ref[t]), 1)

    kernel = functools.partial(
        attend_kernel, key_tile=key_tile, steps=steps, scale=head_dim ** (-0.5))
    return pl.pallas_call(
        kernel,
        out_shape=jax.ShapeDtypeStruct(queries.shape, jnp.bfloat16),
        grid_spec=pltpu.PrefetchScalarGridSpec(
            num_scalar_prefetch=2,
            grid=(models, tiles, steps),
            in_specs=[
                pl.BlockSpec((row_tile, 1), lambda b, t, j, f, l: (t, 0)),
                pl.BlockSpec((row_tile, 1), lambda b, t, j, f, l: (t, 0)),
                pl.BlockSpec((1, row_tile, head_dim), lambda b, t, j, f, l: (b, t, 0)),
                pl.BlockSpec((1, key_tile, head_dim), key_map),
                pl.BlockSpec((1, key_tile, head_dim), value_map),
            ],
            out_specs=pl.BlockSpec((1, row_tile, head_dim), lambda b, t, j, f, l: (b, t, 0)),
            scratch_shapes=[
                pltpu.VMEM((row_tile, 1), jnp.float32),
                pltpu.VMEM((row_tile, 1), jnp.float32),
                pltpu.VMEM((row_tile, head_dim), jnp.float32),
            ],
        ),
        compiler_params=pltpu.CompilerParams(
            dimension_semantics=("arbitrary", "arbitrary", "arbitrary")),
    )(first, last, lo, hi, queries, kv, kv)


def shards(doc_lengths, queries, rotated_key_rows, value_row_matrix):
    models, query_count, feature_width = queries.shape
    kv_heads = rotated_key_rows.shape[2] // HEAD_SIZE
    head_groups = lax.axis_size("head")
    kv_local = kv_heads // head_groups
    local_rows = rotated_key_rows.shape[1]
    paired = jnp.stack(
        [
            rotated_key_rows.reshape(models, local_rows, kv_heads, HEAD_SIZE),
            value_row_matrix.reshape(models, local_rows, kv_heads, HEAD_SIZE),
        ],
        axis=3,
    ).reshape(models, local_rows, kv_heads * 2 * HEAD_SIZE)
    local_kv = lax.all_to_all(paired, "head", split_axis=2, concat_axis=1, tiled=True)
    kv = lax.all_gather(local_kv, "ctx", axis=1, tiled=True)
    assert kv_local == 1

    group_width = feature_width // HEAD_SIZE
    rows = query_count * group_width
    flat_queries = queries.reshape(models, rows, HEAD_SIZE)
    doc_ends = jnp.cumsum(doc_lengths).astype(jnp.int32)
    query_start = lax.axis_index("ctx") * query_count
    row_pos = query_start + jnp.arange(rows, dtype=jnp.int32) // group_width
    row_lo = jnp.max(
        jnp.where(doc_ends[None, :] <= row_pos[:, None], doc_ends[None, :], 0), axis=1)
    row_tile = min(ROW_TILE, rows)
    key_tile = min(KEY_TILE, kv.shape[1])
    first = row_lo[::row_tile] // key_tile
    last = row_pos[row_tile - 1::row_tile] // key_tile
    mixed = attend(
        flat_queries, kv, first, last, row_lo.reshape(rows, 1), row_pos.reshape(rows, 1))
    return mixed.reshape(models, query_count, feature_width)


def solution(mesh):
    placed = (
        P(),
        P(None, "ctx", "head"),
        P(None, ("ctx", "head"), None),
        P(None, ("ctx", "head"), None),
    )
    return jax.shard_map(
        shards, mesh=mesh, in_specs=placed, out_specs=P(None, "ctx", "head"), check_vma=False
    )
```

```python
import functools

import jax
import jax.numpy as jnp
from jax import lax
from jax.experimental import pallas as pl
from jax.experimental.pallas import tpu as pltpu
from jax.sharding import PartitionSpec as P

HEAD_SIZE = 128
LONGEST = 4352
NEG_FILL = -1e30

KEY_TILE = 512


def attend_kernel(meta_ref, lo_ref, hi_ref, q_ref, k_ref, v_ref, *rest,
                  key_tile, steps, scale, heads):
    o_ref, peak_sc, total_sc, accum_sc = rest[-4:]
    step = pl.program_id(0)
    block = meta_ref[0] + step
    key_start = block * key_tile

    @pl.when(step == 0)
    def _():
        peak_sc[...] = jnp.full(peak_sc.shape, NEG_FILL, jnp.float32)
        total_sc[...] = jnp.zeros(total_sc.shape, jnp.float32)
        accum_sc[...] = jnp.zeros(accum_sc.shape, jnp.float32)

    live = block <= meta_ref[1]
    inner = (key_start >= meta_ref[2]) & (key_start + key_tile - 1 <= meta_ref[3])

    def update(masked):
        keys = k_ref[...]
        values = v_ref[...]
        if masked:
            key_pos = key_start + lax.broadcasted_iota(jnp.int32, (1, key_tile), 1)
            allowed = (key_pos >= lo_ref[...]) & (key_pos <= hi_ref[...])
        for h in range(heads):
            cols = slice(h * HEAD_SIZE, (h + 1) * HEAD_SIZE)
            scores = lax.dot_general(
                q_ref[0, :, cols], keys, (((1,), (1,)), ((), ())),
                preferred_element_type=jnp.float32) * scale
            if masked:
                scores = jnp.where(allowed, scores, NEG_FILL)
            peak_old = peak_sc[h]
            peak_new = jnp.maximum(peak_old, jnp.max(scores, axis=-1, keepdims=True))
            probs = jnp.exp(scores - peak_new)
            if masked:
                probs = jnp.where(allowed, probs, 0.0)
            factor = jnp.exp(peak_old - peak_new)
            total_sc[h] = total_sc[h] * factor + jnp.sum(probs, axis=-1, keepdims=True)
            accum_sc[h] = accum_sc[h] * factor + lax.dot_general(
                probs.astype(jnp.bfloat16), values, (((1,), (0,)), ((), ())),
                preferred_element_type=jnp.float32)
            peak_sc[h] = peak_new

    @pl.when(live & inner)
    def _():
        update(False)

    @pl.when(live & jnp.logical_not(inner))
    def _():
        update(True)

    @pl.when(step == steps - 1)
    def _():
        for h in range(heads):
            cols = slice(h * HEAD_SIZE, (h + 1) * HEAD_SIZE)
            o_ref[0, :, cols] = (accum_sc[h] / total_sc[h]).astype(o_ref.dtype)


def attend(model, queries, kv, meta, lo, hi, prior):
    models, query_count, feature_width = queries.shape
    heads = feature_width // HEAD_SIZE
    key_count = kv.shape[0]
    key_tile = min(KEY_TILE, key_count)
    steps = min(key_count // key_tile, (LONGEST + query_count - 2) // key_tile + 2)

    def key_map(j, meta_ref):
        return (jnp.minimum(meta_ref[0] + j, meta_ref[1]), 0)

    def value_map(j, meta_ref):
        return (jnp.minimum(meta_ref[0] + j, meta_ref[1]), 1)

    in_specs = [
        pl.BlockSpec((query_count, 1), lambda j, m: (0, 0)),
        pl.BlockSpec((query_count, 1), lambda j, m: (0, 0)),
        pl.BlockSpec((1, query_count, feature_width), lambda j, m: (model, 0, 0)),
        pl.BlockSpec((key_tile, HEAD_SIZE), key_map),
        pl.BlockSpec((key_tile, HEAD_SIZE), value_map),
    ]
    operands = [meta, lo, hi, queries, kv, kv]
    aliases = {}
    if prior is not None:
        in_specs.append(pl.BlockSpec(memory_space=pl.ANY))
        operands.append(prior)
        aliases = {len(operands) - 1: 0}
    kernel = functools.partial(
        attend_kernel, key_tile=key_tile, steps=steps, scale=HEAD_SIZE ** (-0.5), heads=heads)
    return pl.pallas_call(
        kernel,
        out_shape=jax.ShapeDtypeStruct(queries.shape, jnp.bfloat16),
        grid_spec=pltpu.PrefetchScalarGridSpec(
            num_scalar_prefetch=1,
            grid=(steps,),
            in_specs=in_specs,
            out_specs=pl.BlockSpec((1, query_count, feature_width), lambda j, m: (model, 0, 0)),
            scratch_shapes=[
                pltpu.VMEM((heads, query_count, 1), jnp.float32),
                pltpu.VMEM((heads, query_count, 1), jnp.float32),
                pltpu.VMEM((heads, query_count, HEAD_SIZE), jnp.float32),
            ],
        ),
        input_output_aliases=aliases,
        compiler_params=pltpu.CompilerParams(dimension_semantics=("arbitrary",)),
    )(*operands)


def shards(doc_lengths, queries, rotated_key_rows, value_row_matrix):
    models, query_count, feature_width = queries.shape
    kv_heads = rotated_key_rows.shape[2] // HEAD_SIZE
    head_groups = lax.axis_size("head")
    assert kv_heads == head_groups
    local_rows = rotated_key_rows.shape[1]
    paired = jnp.stack(
        [
            rotated_key_rows.reshape(models, local_rows, kv_heads, HEAD_SIZE),
            value_row_matrix.reshape(models, local_rows, kv_heads, HEAD_SIZE),
        ],
        axis=3,
    ).reshape(models, local_rows, kv_heads * 2 * HEAD_SIZE)
    local_kv = lax.all_to_all(paired, "head", split_axis=2, concat_axis=1, tiled=True)

    doc_ends = jnp.cumsum(doc_lengths).astype(jnp.int32)
    query_start = lax.axis_index("ctx") * query_count
    query_pos = query_start + jnp.arange(query_count, dtype=jnp.int32)
    query_lo = jnp.max(
        jnp.where(doc_ends[None, :] <= query_pos[:, None], doc_ends[None, :], 0), axis=1)
    key_tile = min(KEY_TILE, query_count * lax.axis_size("ctx"))
    meta = jnp.stack([
        query_lo[0] // key_tile,
        query_pos[-1] // key_tile,
        query_lo[-1],
        query_pos[0],
    ]).astype(jnp.int32)
    lo = query_lo.reshape(query_count, 1)
    hi = query_pos.reshape(query_count, 1)

    out = None
    for model in range(models):
        kv = lax.all_gather(local_kv[model], "ctx", axis=0, tiled=True)
        out = attend(model, queries, kv, meta, lo, hi, out)
    return out


def solution(mesh):
    placed = (
        P(),
        P(None, "ctx", "head"),
        P(None, ("ctx", "head"), None),
        P(None, ("ctx", "head"), None),
    )
    return jax.shard_map(
        shards, mesh=mesh, in_specs=placed, out_specs=P(None, "ctx", "head"), check_vma=False
    )
```

```python
import functools

import jax
import jax.numpy as jnp
from jax import lax
from jax.experimental import pallas as pl
from jax.experimental.pallas import tpu as pltpu
from jax.sharding import PartitionSpec as P

HEAD_SIZE = 128
LONGEST = 4352
NEG_FILL = -1e30

KEY_TILE = 512
STAT_LANES = 128
LOG2E = 1.4426950408889634


def attend_kernel(meta_ref, lo_ref, hi_ref, q_ref, k_ref, v_ref, o_ref,
                  peak_sc, total_sc, accum_sc, *, key_tile, steps, scale, heads):
    step = pl.program_id(1)
    block = meta_ref[0] + step
    key_start = block * key_tile

    @pl.when(step == 0)
    def _():
        peak_sc[...] = jnp.full(peak_sc.shape, NEG_FILL, jnp.float32)
        total_sc[...] = jnp.zeros(total_sc.shape, jnp.float32)
        accum_sc[...] = jnp.zeros(accum_sc.shape, jnp.float32)

    live = block <= meta_ref[1]
    inner = (key_start >= meta_ref[2]) & (key_start + key_tile - 1 <= meta_ref[3])
    reps = key_tile // STAT_LANES

    def update(masked):
        keys = k_ref[0]
        values = v_ref[0]
        if masked:
            key_pos = key_start + lax.broadcasted_iota(jnp.int32, (1, key_tile), 1)
            allowed = (key_pos >= lo_ref[...]) & (key_pos <= hi_ref[...])
        for h in range(heads):
            cols = slice(h * HEAD_SIZE, (h + 1) * HEAD_SIZE)
            scores = lax.dot_general(
                q_ref[0, :, cols], keys, (((1,), (1,)), ((), ())),
                preferred_element_type=jnp.float32)
            if masked:
                scores = jnp.where(allowed, scores, NEG_FILL)
            peak_old = peak_sc[h]
            peak_new = jnp.maximum(peak_old, jnp.max(scores, axis=-1, keepdims=True))
            shift = peak_new * scale
            probs = jnp.exp2(scores * scale - jnp.tile(shift, (1, reps)))
            if masked:
                probs = jnp.where(allowed, probs, 0.0)
            factor = jnp.exp2(peak_old * scale - shift)
            total_sc[h] = total_sc[h] * factor + jnp.sum(probs, axis=-1, keepdims=True)
            accum_sc[h] = accum_sc[h] * factor + lax.dot_general(
                probs.astype(jnp.bfloat16), values, (((1,), (0,)), ((), ())),
                preferred_element_type=jnp.float32)
            peak_sc[h] = peak_new

    @pl.when(live & inner)
    def _():
        update(False)

    @pl.when(live & jnp.logical_not(inner))
    def _():
        update(True)

    @pl.when(step == steps - 1)
    def _():
        for h in range(heads):
            cols = slice(h * HEAD_SIZE, (h + 1) * HEAD_SIZE)
            o_ref[0, :, cols] = (accum_sc[h] / total_sc[h]).astype(o_ref.dtype)


def attend(queries, kv, meta, lo, hi):
    models, query_count, feature_width = queries.shape
    heads = feature_width // HEAD_SIZE
    key_count = kv.shape[1]
    key_tile = min(KEY_TILE, key_count)
    steps = min(key_count // key_tile, (LONGEST + query_count - 2) // key_tile + 2)

    def key_map(b, j, meta_ref):
        return (b, jnp.minimum(meta_ref[0] + j, meta_ref[1]), 0)

    def value_map(b, j, meta_ref):
        return (b, jnp.minimum(meta_ref[0] + j, meta_ref[1]), 1)

    kernel = functools.partial(
        attend_kernel, key_tile=key_tile, steps=steps,
        scale=HEAD_SIZE ** (-0.5) * LOG2E, heads=heads)
    return pl.pallas_call(
        kernel,
        out_shape=jax.ShapeDtypeStruct(queries.shape, jnp.bfloat16),
        grid_spec=pltpu.PrefetchScalarGridSpec(
            num_scalar_prefetch=1,
            grid=(models, steps),
            in_specs=[
                pl.BlockSpec((query_count, 1), lambda b, j, m: (0, 0)),
                pl.BlockSpec((query_count, 1), lambda b, j, m: (0, 0)),
                pl.BlockSpec((1, query_count, feature_width), lambda b, j, m: (b, 0, 0)),
                pl.BlockSpec((1, key_tile, HEAD_SIZE), key_map),
                pl.BlockSpec((1, key_tile, HEAD_SIZE), value_map),
            ],
            out_specs=pl.BlockSpec((1, query_count, feature_width), lambda b, j, m: (b, 0, 0)),
            scratch_shapes=[
                pltpu.VMEM((heads, query_count, STAT_LANES), jnp.float32),
                pltpu.VMEM((heads, query_count, STAT_LANES), jnp.float32),
                pltpu.VMEM((heads, query_count, HEAD_SIZE), jnp.float32),
            ],
        ),
        compiler_params=pltpu.CompilerParams(dimension_semantics=("arbitrary", "arbitrary")),
    )(meta, lo, hi, queries, kv, kv)


def shards(doc_lengths, queries, rotated_key_rows, value_row_matrix):
    models, query_count, feature_width = queries.shape
    kv_heads = rotated_key_rows.shape[2] // HEAD_SIZE
    head_groups = lax.axis_size("head")
    assert kv_heads == head_groups
    local_rows = rotated_key_rows.shape[1]
    paired = jnp.stack(
        [
            rotated_key_rows.reshape(models, local_rows, kv_heads, HEAD_SIZE),
            value_row_matrix.reshape(models, local_rows, kv_heads, HEAD_SIZE),
        ],
        axis=3,
    ).reshape(models, local_rows, kv_heads * 2 * HEAD_SIZE)
    local_kv = lax.all_to_all(paired, "head", split_axis=2, concat_axis=1, tiled=True)

    doc_ends = jnp.cumsum(doc_lengths).astype(jnp.int32)
    query_start = lax.axis_index("ctx") * query_count
    query_pos = query_start + jnp.arange(query_count, dtype=jnp.int32)
    query_lo = jnp.max(
        jnp.where(doc_ends[None, :] <= query_pos[:, None], doc_ends[None, :], 0), axis=1)
    key_tile = min(KEY_TILE, query_count * lax.axis_size("ctx"))
    meta = jnp.stack([
        query_lo[0] // key_tile,
        query_pos[-1] // key_tile,
        query_lo[-1],
        query_pos[0],
    ]).astype(jnp.int32)
    lo = query_lo.reshape(query_count, 1)
    hi = query_pos.reshape(query_count, 1)

    kv = lax.all_gather(local_kv, "ctx", axis=1, tiled=True)
    return attend(queries, kv, meta, lo, hi)


def solution(mesh):
    placed = (
        P(),
        P(None, "ctx", "head"),
        P(None, ("ctx", "head"), None),
        P(None, ("ctx", "head"), None),
    )
    return jax.shard_map(
        shards, mesh=mesh, in_specs=placed, out_specs=P(None, "ctx", "head"), check_vma=False
    )
```

```python
import functools

import jax
import jax.numpy as jnp
from jax import lax
from jax.experimental import pallas as pl
from jax.experimental.pallas import tpu as pltpu
from jax.sharding import PartitionSpec as P


HEAD_SIZE = 128
LONGEST = 4352
NEG_FILL = -1e30

KEY_TILE = 512
STAT_LANES = 128
LOG2E = 1.4426950408889634
NEAR_BLOCKS = 3


def attend_kernel(meta_ref, lo_ref, hi_ref, q_ref, k_ref, v_ref, *rest,
                  key_tile, steps, scale, heads, resume, finish):
    if resume:
        peak_in, total_in, accum_in = rest[:3]
        rest = rest[3:]
    if finish:
        o_ref, peak_sc, total_sc, accum_sc = rest
    else:
        peak_out, total_out, accum_out, peak_sc, total_sc, accum_sc = rest
    step = pl.program_id(1)
    block = meta_ref[0] + step
    key_start = meta_ref[4] + block * key_tile

    @pl.when(step == 0)
    def _():
        if resume:
            peak_sc[...] = peak_in[0]
            total_sc[...] = total_in[0]
            accum_sc[...] = accum_in[0]
        else:
            peak_sc[...] = jnp.full(peak_sc.shape, NEG_FILL, jnp.float32)
            total_sc[...] = jnp.zeros(total_sc.shape, jnp.float32)
            accum_sc[...] = jnp.zeros(accum_sc.shape, jnp.float32)

    live = block <= meta_ref[1]
    inner = (key_start >= meta_ref[2]) & (key_start + key_tile - 1 <= meta_ref[3])
    reps = key_tile // STAT_LANES

    def update(masked):
        keys = k_ref[0]
        values = v_ref[0]
        if masked:
            key_pos = key_start + lax.broadcasted_iota(jnp.int32, (1, key_tile), 1)
            allowed = (key_pos >= lo_ref[...]) & (key_pos <= hi_ref[...])
        for h in range(heads):
            cols = slice(h * HEAD_SIZE, (h + 1) * HEAD_SIZE)
            scores = lax.dot_general(
                q_ref[0, :, cols], keys, (((1,), (1,)), ((), ())),
                preferred_element_type=jnp.float32)
            if masked:
                scores = jnp.where(allowed, scores, NEG_FILL)
            peak_old = peak_sc[h]
            peak_new = jnp.maximum(peak_old, jnp.max(scores, axis=-1, keepdims=True))
            shift = peak_new * scale
            probs = jnp.exp2(scores * scale - jnp.tile(shift, (1, reps)))
            if masked:
                probs = jnp.where(allowed, probs, 0.0)
            factor = jnp.exp2(peak_old * scale - shift)
            total_sc[h] = total_sc[h] * factor + jnp.sum(probs, axis=-1, keepdims=True)
            accum_sc[h] = accum_sc[h] * factor + lax.dot_general(
                probs.astype(jnp.bfloat16), values, (((1,), (0,)), ((), ())),
                preferred_element_type=jnp.float32)
            peak_sc[h] = peak_new

    @pl.when(live & inner)
    def _():
        update(False)

    @pl.when(live & jnp.logical_not(inner))
    def _():
        update(True)

    @pl.when(step == steps - 1)
    def _():
        if finish:
            for h in range(heads):
                cols = slice(h * HEAD_SIZE, (h + 1) * HEAD_SIZE)
                o_ref[0, :, cols] = (accum_sc[h] / total_sc[h]).astype(o_ref.dtype)
        else:
            peak_out[0] = peak_sc[...]
            total_out[0] = total_sc[...]
            accum_out[0] = accum_sc[...]


def attend(queries, kv, meta, lo, hi, state, steps_cap):
    models, query_count, feature_width = queries.shape
    heads = feature_width // HEAD_SIZE
    key_count = kv.shape[1]
    key_tile = min(KEY_TILE, key_count)
    steps = min(key_count // key_tile, steps_cap)
    resume = state is not None
    finish = resume

    def key_map(b, j, meta_ref):
        return (b, jnp.maximum(jnp.minimum(meta_ref[0] + j, meta_ref[1]), 0), 0)

    def value_map(b, j, meta_ref):
        return (b, jnp.maximum(jnp.minimum(meta_ref[0] + j, meta_ref[1]), 0), 1)

    stat_shape = (models, heads, query_count, STAT_LANES)
    stat_spec = pl.BlockSpec((1, heads, query_count, STAT_LANES), lambda b, j, m: (b, 0, 0, 0))
    in_specs = [
        pl.BlockSpec((query_count, 1), lambda b, j, m: (0, 0)),
        pl.BlockSpec((query_count, 1), lambda b, j, m: (0, 0)),
        pl.BlockSpec((1, query_count, feature_width), lambda b, j, m: (b, 0, 0)),
        pl.BlockSpec((1, key_tile, HEAD_SIZE), key_map),
        pl.BlockSpec((1, key_tile, HEAD_SIZE), value_map),
    ]
    operands = [meta, lo, hi, queries, kv, kv]
    if resume:
        in_specs += [stat_spec] * 3
        operands += list(state)
    if finish:
        out_shape = jax.ShapeDtypeStruct(queries.shape, jnp.bfloat16)
        out_specs = pl.BlockSpec((1, query_count, feature_width), lambda b, j, m: (b, 0, 0))
    else:
        out_shape = [jax.ShapeDtypeStruct(stat_shape, jnp.float32)] * 3
        out_specs = [stat_spec] * 3

    kernel = functools.partial(
        attend_kernel, key_tile=key_tile, steps=steps,
        scale=HEAD_SIZE ** (-0.5) * LOG2E, heads=heads, resume=resume, finish=finish)
    return pl.pallas_call(
        kernel,
        out_shape=out_shape,
        grid_spec=pltpu.PrefetchScalarGridSpec(
            num_scalar_prefetch=1,
            grid=(models, steps),
            in_specs=in_specs,
            out_specs=out_specs,
            scratch_shapes=[
                pltpu.VMEM((heads, query_count, STAT_LANES), jnp.float32),
                pltpu.VMEM((heads, query_count, STAT_LANES), jnp.float32),
                pltpu.VMEM((heads, query_count, HEAD_SIZE), jnp.float32),
            ],
        ),
        compiler_params=pltpu.CompilerParams(dimension_semantics=("arbitrary", "arbitrary")),
    )(*operands)


def layer(doc_lengths, queries, rotated_key_rows, value_row_matrix):
    models, query_count, _ = queries.shape
    kv_heads = rotated_key_rows.shape[2] // HEAD_SIZE
    head_groups = lax.axis_size("head")
    assert kv_heads == head_groups
    local_rows = rotated_key_rows.shape[1]
    paired = jnp.stack(
        [
            rotated_key_rows.reshape(models, local_rows, kv_heads, HEAD_SIZE),
            value_row_matrix.reshape(models, local_rows, kv_heads, HEAD_SIZE),
        ],
        axis=3,
    ).reshape(models, local_rows, kv_heads * 2 * HEAD_SIZE)
    local_kv = lax.all_to_all(paired, "head", split_axis=2, concat_axis=1, tiled=True)

    ctx_size = lax.axis_size("ctx")
    near_kv = jnp.concatenate(
        [
            lax.ppermute(local_kv, "ctx", [(i, i + k) for i in range(ctx_size - k)])
            for k in range(NEAR_BLOCKS, 0, -1)
        ]
        + [local_kv],
        axis=1,
    )
    kv = lax.all_gather(local_kv, "ctx", axis=1, tiled=True)

    doc_ends = jnp.cumsum(doc_lengths).astype(jnp.int32)
    query_start = lax.axis_index("ctx") * query_count
    query_pos = query_start + jnp.arange(query_count, dtype=jnp.int32)
    query_lo = jnp.max(
        jnp.where(doc_ends[None, :] <= query_pos[:, None], doc_ends[None, :], 0), axis=1)
    key_tile = min(KEY_TILE, query_count * ctx_size)
    near_start = query_start - NEAR_BLOCKS * query_count
    near_meta = jnp.stack([
        jnp.maximum(query_lo[0] - near_start, 0) // key_tile,
        (query_pos[-1] - near_start) // key_tile,
        query_lo[-1],
        query_pos[0],
        near_start,
    ]).astype(jnp.int32)
    far_hi = jnp.minimum(query_pos, near_start - 1)
    far_meta = jnp.stack([
        query_lo[0] // key_tile,
        jnp.where(near_start > 0, (near_start - 1) // key_tile, -1),
        query_lo[-1],
        far_hi[0],
        0,
    ]).astype(jnp.int32)
    lo = query_lo.reshape(query_count, 1)
    state = attend(queries, near_kv, near_meta, lo, query_pos.reshape(query_count, 1), None,
                   near_kv.shape[1] // key_tile)
    return attend(queries, kv, far_meta, lo, far_hi.reshape(query_count, 1), state,
                  (LONGEST + query_count - 2) // key_tile + 2)


def solution(mesh):
    placed = (
        P(),
        P(None, "ctx", "head"),
        P(None, ("ctx", "head"), None),
        P(None, ("ctx", "head"), None),
    )
    return jax.shard_map(
        layer, mesh=mesh, in_specs=placed, out_specs=P(None, "ctx", "head"), check_vma=False
    )
```

```python
import functools

import jax
import jax.numpy as jnp
from jax import lax
from jax.experimental import pallas as pl
from jax.experimental.pallas import tpu as pltpu
from jax.sharding import PartitionSpec as P


HEAD_SIZE = 128
LONGEST = 4352
NEG_FILL = -1e30

KEY_TILE = 1024
STAT_LANES = 128
LOG2E = 1.4426950408889634
NEAR_BLOCKS = 7


def attend_kernel(meta_ref, lo_ref, hi_ref, q_ref, k_ref, v_ref, *rest,
                  key_tile, steps, scale, heads, resume, finish):
    if resume:
        peak_in, total_in, accum_in = rest[:3]
        rest = rest[3:]
    if finish:
        o_ref, peak_sc, total_sc, accum_sc = rest
    else:
        peak_out, total_out, accum_out, peak_sc, total_sc, accum_sc = rest
    step = pl.program_id(1)
    block = meta_ref[0] + step
    key_start = meta_ref[4] + block * key_tile

    @pl.when(step == 0)
    def _():
        if resume:
            peak_sc[...] = peak_in[0]
            total_sc[...] = total_in[0]
            accum_sc[...] = accum_in[0]
        else:
            peak_sc[...] = jnp.full(peak_sc.shape, NEG_FILL, jnp.float32)
            total_sc[...] = jnp.zeros(total_sc.shape, jnp.float32)
            accum_sc[...] = jnp.zeros(accum_sc.shape, jnp.float32)

    live = block <= meta_ref[1]
    inner = (key_start >= meta_ref[2]) & (key_start + key_tile - 1 <= meta_ref[3])
    reps = key_tile // STAT_LANES

    def update(masked):
        keys = k_ref[0]
        values = v_ref[0]
        if masked:
            key_pos = key_start + lax.broadcasted_iota(jnp.int32, (1, key_tile), 1)
            allowed = (key_pos >= lo_ref[...]) & (key_pos <= hi_ref[...])

        def head_step(h, cols):
            scores = lax.dot_general(
                q_ref[0, :, cols], keys, (((1,), (1,)), ((), ())),
                preferred_element_type=jnp.float32)
            if masked:
                scores = jnp.where(allowed, scores, NEG_FILL)
            peak_old = peak_sc[h]
            peak_new = jnp.maximum(peak_old, jnp.max(scores, axis=-1, keepdims=True))
            shift = peak_new * scale
            probs = jnp.exp2(scores * scale - jnp.tile(shift, (1, reps)))
            if masked:
                probs = jnp.where(allowed, probs, 0.0)
            factor = jnp.exp2(peak_old * scale - shift)
            total_sc[h] = total_sc[h] * factor + jnp.sum(probs, axis=-1, keepdims=True)
            accum_sc[h] = accum_sc[h] * factor + lax.dot_general(
                probs.astype(jnp.bfloat16), values, (((1,), (0,)), ((), ())),
                preferred_element_type=jnp.float32)
            peak_sc[h] = peak_new

        if masked:
            def body(h, carry):
                head_step(h, pl.ds(pl.multiple_of(h * HEAD_SIZE, HEAD_SIZE), HEAD_SIZE))
                return carry

            lax.fori_loop(0, heads, body, 0)
        else:
            for h in range(heads):
                head_step(h, slice(h * HEAD_SIZE, (h + 1) * HEAD_SIZE))

    @pl.when(live & inner)
    def _():
        update(False)

    @pl.when(live & jnp.logical_not(inner))
    def _():
        update(True)

    @pl.when(step == steps - 1)
    def _():
        if finish:
            for h in range(heads):
                cols = slice(h * HEAD_SIZE, (h + 1) * HEAD_SIZE)
                o_ref[0, :, cols] = (accum_sc[h] / total_sc[h]).astype(o_ref.dtype)
        else:
            peak_out[0] = peak_sc[...]
            total_out[0] = total_sc[...]
            accum_out[0] = accum_sc[...]


def attend(queries, kv, meta, lo, hi, state, steps_cap):
    models, query_count, feature_width = queries.shape
    heads = feature_width // HEAD_SIZE
    key_count = kv.shape[1]
    key_tile = min(KEY_TILE, key_count)
    steps = min(key_count // key_tile, steps_cap)
    resume = state is not None
    finish = resume

    def key_map(b, j, meta_ref):
        return (b, jnp.maximum(jnp.minimum(meta_ref[0] + j, meta_ref[1]), 0), 0)

    def value_map(b, j, meta_ref):
        return (b, jnp.maximum(jnp.minimum(meta_ref[0] + j, meta_ref[1]), 0), 1)

    stat_shape = (models, heads, query_count, STAT_LANES)
    stat_spec = pl.BlockSpec((1, heads, query_count, STAT_LANES), lambda b, j, m: (b, 0, 0, 0))
    in_specs = [
        pl.BlockSpec((query_count, 1), lambda b, j, m: (0, 0)),
        pl.BlockSpec((query_count, 1), lambda b, j, m: (0, 0)),
        pl.BlockSpec((1, query_count, feature_width), lambda b, j, m: (b, 0, 0)),
        pl.BlockSpec((1, key_tile, HEAD_SIZE), key_map),
        pl.BlockSpec((1, key_tile, HEAD_SIZE), value_map),
    ]
    operands = [meta, lo, hi, queries, kv, kv]
    if resume:
        in_specs += [stat_spec] * 3
        operands += list(state)
    if finish:
        out_shape = jax.ShapeDtypeStruct(queries.shape, jnp.bfloat16)
        out_specs = pl.BlockSpec((1, query_count, feature_width), lambda b, j, m: (b, 0, 0))
    else:
        out_shape = [jax.ShapeDtypeStruct(stat_shape, jnp.float32)] * 3
        out_specs = [stat_spec] * 3

    kernel = functools.partial(
        attend_kernel, key_tile=key_tile, steps=steps,
        scale=HEAD_SIZE ** (-0.5) * LOG2E, heads=heads, resume=resume, finish=finish)
    return pl.pallas_call(
        kernel,
        out_shape=out_shape,
        grid_spec=pltpu.PrefetchScalarGridSpec(
            num_scalar_prefetch=1,
            grid=(models, steps),
            in_specs=in_specs,
            out_specs=out_specs,
            scratch_shapes=[
                pltpu.VMEM((heads, query_count, STAT_LANES), jnp.float32),
                pltpu.VMEM((heads, query_count, STAT_LANES), jnp.float32),
                pltpu.VMEM((heads, query_count, HEAD_SIZE), jnp.float32),
            ],
        ),
        compiler_params=pltpu.CompilerParams(dimension_semantics=("arbitrary", "arbitrary")),
    )(*operands)


def layer(doc_lengths, queries, rotated_key_rows, value_row_matrix):
    models, query_count, _ = queries.shape
    kv_heads = rotated_key_rows.shape[2] // HEAD_SIZE
    head_groups = lax.axis_size("head")
    assert kv_heads == head_groups
    local_rows = rotated_key_rows.shape[1]
    paired = jnp.stack(
        [
            rotated_key_rows.reshape(models, local_rows, kv_heads, HEAD_SIZE),
            value_row_matrix.reshape(models, local_rows, kv_heads, HEAD_SIZE),
        ],
        axis=3,
    ).reshape(models, local_rows, kv_heads * 2 * HEAD_SIZE)
    local_kv = lax.all_to_all(paired, "head", split_axis=2, concat_axis=1, tiled=True)

    ctx_size = lax.axis_size("ctx")
    near_kv = jnp.concatenate(
        [
            lax.ppermute(local_kv, "ctx", [(i, i + k) for i in range(ctx_size - k)])
            for k in range(NEAR_BLOCKS, 0, -1)
        ]
        + [local_kv],
        axis=1,
    )
    kv = lax.all_gather(local_kv, "ctx", axis=1, tiled=True)

    doc_ends = jnp.cumsum(doc_lengths).astype(jnp.int32)
    query_start = lax.axis_index("ctx") * query_count
    query_pos = query_start + jnp.arange(query_count, dtype=jnp.int32)
    query_lo = jnp.max(
        jnp.where(doc_ends[None, :] <= query_pos[:, None], doc_ends[None, :], 0), axis=1)
    key_tile = min(KEY_TILE, query_count * ctx_size)
    near_start = query_start - NEAR_BLOCKS * query_count
    near_meta = jnp.stack([
        jnp.maximum(query_lo[0] - near_start, 0) // key_tile,
        (query_pos[-1] - near_start) // key_tile,
        query_lo[-1],
        query_pos[0],
        near_start,
    ]).astype(jnp.int32)
    far_hi = jnp.minimum(query_pos, near_start - 1)
    far_meta = jnp.stack([
        query_lo[0] // key_tile,
        jnp.where(near_start > 0, (near_start - 1) // key_tile, -1),
        query_lo[-1],
        far_hi[0],
        0,
    ]).astype(jnp.int32)
    lo = query_lo.reshape(query_count, 1)
    state = attend(queries, near_kv, near_meta, lo, query_pos.reshape(query_count, 1), None,
                   near_kv.shape[1] // key_tile)
    return attend(queries, kv, far_meta, lo, far_hi.reshape(query_count, 1), state,
                  max(1, (LONGEST - 1 - NEAR_BLOCKS * query_count) // key_tile + 2))


def solution(mesh):
    placed = (
        P(),
        P(None, "ctx", "head"),
        P(None, ("ctx", "head"), None),
        P(None, ("ctx", "head"), None),
    )
    return jax.shard_map(
        layer, mesh=mesh, in_specs=placed, out_specs=P(None, "ctx", "head"), check_vma=False
    )
```

```python
import functools

import jax
import jax.numpy as jnp
from jax import lax
from jax.experimental import pallas as pl
from jax.experimental.pallas import tpu as pltpu
from jax.sharding import PartitionSpec as P


HEAD_SIZE = 128
LONGEST = 4352
NEG_FILL = -1e30

KEY_TILE = 512
STAT_LANES = 128
LOG2E = 1.4426950408889634
NEAR_BLOCKS = 5


def attend_kernel(meta_ref, lo_ref, hi_ref, q_ref, k_ref, v_ref, *rest,
                  key_tile, steps, scale, heads, resume, finish):
    if resume:
        peak_in, total_in, accum_in = rest[:3]
        rest = rest[3:]
    if finish:
        o_ref, peak_sc, total_sc, accum_sc = rest
    else:
        peak_out, total_out, accum_out, peak_sc, total_sc, accum_sc = rest
    step = pl.program_id(1)
    block = meta_ref[0] + step
    key_start = meta_ref[4] + block * key_tile

    @pl.when(step == 0)
    def _():
        if resume:
            peak_sc[...] = peak_in[0]
            total_sc[...] = total_in[0]
            accum_sc[...] = accum_in[0]
        else:
            peak_sc[...] = jnp.full(peak_sc.shape, NEG_FILL, jnp.float32)
            total_sc[...] = jnp.zeros(total_sc.shape, jnp.float32)
            accum_sc[...] = jnp.zeros(accum_sc.shape, jnp.float32)

    live = block <= meta_ref[1]
    inner = (key_start >= meta_ref[2]) & (key_start + key_tile - 1 <= meta_ref[3])
    reps = key_tile // STAT_LANES

    def update(masked):
        keys = k_ref[0]
        values = v_ref[0]
        if masked:
            key_pos = key_start + lax.broadcasted_iota(jnp.int32, (1, key_tile), 1)
            allowed = (key_pos >= lo_ref[...]) & (key_pos <= hi_ref[...])
        for h in range(heads):
            cols = slice(h * HEAD_SIZE, (h + 1) * HEAD_SIZE)
            scores = lax.dot_general(
                q_ref[0, :, cols], keys, (((1,), (1,)), ((), ())),
                preferred_element_type=jnp.float32)
            if masked:
                scores = jnp.where(allowed, scores, NEG_FILL)
            peak_old = peak_sc[h]
            peak_new = jnp.maximum(peak_old, jnp.max(scores, axis=-1, keepdims=True))
            shift = peak_new * scale
            probs = jnp.exp2(scores * scale - jnp.tile(shift, (1, reps)))
            factor = jnp.exp2(peak_old * scale - shift)
            total_sc[h] = total_sc[h] * factor + jnp.sum(probs, axis=-1, keepdims=True)
            accum_sc[h] = accum_sc[h] * factor + lax.dot_general(
                probs.astype(jnp.bfloat16), values, (((1,), (0,)), ((), ())),
                preferred_element_type=jnp.float32)
            peak_sc[h] = peak_new

    @pl.when(live & inner)
    def _():
        update(False)

    @pl.when(live & jnp.logical_not(inner))
    def _():
        update(True)

    @pl.when(step == steps - 1)
    def _():
        if finish:
            for h in range(heads):
                cols = slice(h * HEAD_SIZE, (h + 1) * HEAD_SIZE)
                o_ref[0, :, cols] = (accum_sc[h] / total_sc[h]).astype(o_ref.dtype)
        else:
            peak_out[0] = peak_sc[...]
            total_out[0] = total_sc[...]
            accum_out[0] = accum_sc[...]


def attend(queries, kv, meta, lo, hi, state, steps_cap):
    models, query_count, feature_width = queries.shape
    heads = feature_width // HEAD_SIZE
    key_count = kv.shape[1]
    key_tile = min(KEY_TILE, key_count)
    steps = min(key_count // key_tile, steps_cap)
    resume = state is not None
    finish = resume

    def key_map(b, j, meta_ref):
        return (b, jnp.maximum(jnp.minimum(meta_ref[0] + j, meta_ref[1]), 0), 0)

    def value_map(b, j, meta_ref):
        return (b, jnp.maximum(jnp.minimum(meta_ref[0] + j, meta_ref[1]), 0), 1)

    stat_shape = (models, heads, query_count, STAT_LANES)
    stat_spec = pl.BlockSpec((1, heads, query_count, STAT_LANES), lambda b, j, m: (b, 0, 0, 0))
    in_specs = [
        pl.BlockSpec((query_count, 1), lambda b, j, m: (0, 0)),
        pl.BlockSpec((query_count, 1), lambda b, j, m: (0, 0)),
        pl.BlockSpec((1, query_count, feature_width), lambda b, j, m: (b, 0, 0)),
        pl.BlockSpec((1, key_tile, HEAD_SIZE), key_map),
        pl.BlockSpec((1, key_tile, HEAD_SIZE), value_map),
    ]
    operands = [meta, lo, hi, queries, kv, kv]
    if resume:
        in_specs += [stat_spec] * 3
        operands += list(state)
    if finish:
        out_shape = jax.ShapeDtypeStruct(queries.shape, jnp.bfloat16)
        out_specs = pl.BlockSpec((1, query_count, feature_width), lambda b, j, m: (b, 0, 0))
    else:
        out_shape = [jax.ShapeDtypeStruct(stat_shape, jnp.float32)] * 3
        out_specs = [stat_spec] * 3

    kernel = functools.partial(
        attend_kernel, key_tile=key_tile, steps=steps,
        scale=HEAD_SIZE ** (-0.5) * LOG2E, heads=heads, resume=resume, finish=finish)
    return pl.pallas_call(
        kernel,
        out_shape=out_shape,
        grid_spec=pltpu.PrefetchScalarGridSpec(
            num_scalar_prefetch=1,
            grid=(models, steps),
            in_specs=in_specs,
            out_specs=out_specs,
            scratch_shapes=[
                pltpu.VMEM((heads, query_count, STAT_LANES), jnp.float32),
                pltpu.VMEM((heads, query_count, STAT_LANES), jnp.float32),
                pltpu.VMEM((heads, query_count, HEAD_SIZE), jnp.float32),
            ],
        ),
        compiler_params=pltpu.CompilerParams(dimension_semantics=("arbitrary", "arbitrary")),
    )(*operands)


def layer(doc_lengths, queries, rotated_key_rows, value_row_matrix):
    models, query_count, _ = queries.shape
    kv_heads = rotated_key_rows.shape[2] // HEAD_SIZE
    head_groups = lax.axis_size("head")
    assert kv_heads == head_groups
    local_rows = rotated_key_rows.shape[1]
    paired = jnp.stack(
        [
            rotated_key_rows.reshape(models, local_rows, kv_heads, HEAD_SIZE),
            value_row_matrix.reshape(models, local_rows, kv_heads, HEAD_SIZE),
        ],
        axis=3,
    ).reshape(models, local_rows, kv_heads * 2 * HEAD_SIZE)
    local_kv = lax.all_to_all(paired, "head", split_axis=2, concat_axis=1, tiled=True)

    ctx_size = lax.axis_size("ctx")
    near_kv = jnp.concatenate(
        [
            lax.ppermute(local_kv, "ctx", [(i, i + k) for i in range(ctx_size - k)])
            for k in range(NEAR_BLOCKS, 0, -1)
        ]
        + [local_kv],
        axis=1,
    )
    kv = lax.all_gather(local_kv, "ctx", axis=1, tiled=True)

    doc_ends = jnp.cumsum(doc_lengths).astype(jnp.int32)
    query_start = lax.axis_index("ctx") * query_count
    query_pos = query_start + jnp.arange(query_count, dtype=jnp.int32)
    query_lo = jnp.max(
        jnp.where(doc_ends[None, :] <= query_pos[:, None], doc_ends[None, :], 0), axis=1)
    key_tile = min(KEY_TILE, query_count * ctx_size)
    near_start = query_start - NEAR_BLOCKS * query_count
    near_meta = jnp.stack([
        jnp.maximum(query_lo[0] - near_start, 0) // key_tile,
        (query_pos[-1] - near_start) // key_tile,
        query_lo[-1],
        query_pos[0],
        near_start,
    ]).astype(jnp.int32)
    far_hi = jnp.minimum(query_pos, near_start - 1)
    far_meta = jnp.stack([
        query_lo[0] // key_tile,
        jnp.where(near_start > 0, (near_start - 1) // key_tile, -1),
        query_lo[-1],
        far_hi[0],
        0,
    ]).astype(jnp.int32)
    lo = query_lo.reshape(query_count, 1)
    state = attend(queries, near_kv, near_meta, lo, query_pos.reshape(query_count, 1), None,
                   near_kv.shape[1] // key_tile)
    return attend(queries, kv, far_meta, lo, far_hi.reshape(query_count, 1), state,
                  max(1, (LONGEST - 1 - NEAR_BLOCKS * query_count) // key_tile + 2))


def solution(mesh):
    placed = (
        P(),
        P(None, "ctx", "head"),
        P(None, ("ctx", "head"), None),
        P(None, ("ctx", "head"), None),
    )
    return jax.shard_map(
        layer, mesh=mesh, in_specs=placed, out_specs=P(None, "ctx", "head"), check_vma=False
    )
```
